256 devices in a mesh: pipe: 2 (over core), expert: 128 (over x, z, y).
Axes of the slice: x: 4, y: 4, z: 8, core: 2. Of those that a mesh axis runs over, the one named last changes fastest.
Arguments:
- section_inputs: bfloat16 [2, 16384, 7168], P('pipe', 'expert'), may hold values from -6 to 6
- output_grads: bfloat16 [2, 16384, 7168], P('pipe', 'expert'), may hold values from -6 to 6
- w_gate: bfloat16 [2, 7168, 16384], P('pipe', None, 'expert'), may hold values from -0.0625 to 0.0625
- w_up: bfloat16 [2, 7168, 16384], P('pipe', None, 'expert'), may hold values from -0.0625 to 0.0625
- w_down: bfloat16 [2, 16384, 7168], P('pipe', 'expert'), may hold values from -0.125 to 0.125
- route_ids: int32 [2, 16384, 8], P('pipe', 'expert'), may hold values from 0 to 255, all different within a row; in each aligned block of 128 rows (0 to 127, 128 to 255, ..., all dimensions but the last counted through in order) at most 5 rows name the same one
- route_gates: float32 [2, 16384, 8], P('pipe', 'expert'), may hold values from 0.25 to 1
Outputs:
- handed_grads: bfloat16 [2, 16384, 7168], P('pipe', 'expert')
- down_grads: bfloat16 [2, 16384, 7168], P('pipe', 'expert')
The draws below stay inside these ranges and needn't reach their ends.
Inputs may be any that keep to these rules, and one draw needn't show every extreme that they name: `route_ids`: each row names 8 different experts. Within the 128 rows of one device of one section, no expert is named by more than 5 rows.
All inputs are finite; a program needn't handle non-finite values.
Results may differ from the reference program's by a relative error of at most 0.0057.
Values may be sent and summed in bfloat16 or wider, within the bound.
No kernel may reach another device: no remote copies, remote signals or barrier semaphores. Data moves between devices by JAX's collectives and lax.ppermute only.
A program may use at most 192 MiB of HBM per device.

```python
import math
import jax
import jax.numpy as jnp
import numpy as np
from jax import lax

D = 7168
FF = 2048
EXPERTS = 256
TOPK = 8
SHARDS = 16
TOK_DEV = 128
CAP = 5
LIVE = 8
TOKENS = 16384
N_EXPERT = 128


def steps_of(rng, extent, pieces, least, high):
    level, own = 1.0, jax.random.fold_in(rng, 6)
    for position, shards_of in pieces:
        draws = jnp.exp(jax.random.uniform(jax.random.fold_in(own, position), (shards_of,), jnp.float32, least / len(pieces), high / len(pieces)))
        level = level * jnp.repeat(draws, extent[position] // shards_of).reshape([-1 if axis == position else 1 for axis in range(len(extent))])
    return level


def assign_block(rng, own, number, rows, number_of, top, reach, lean):
    ranking = jax.random.permutation(rng, number_of)
    crowded, usual = shares(number_of, rows * top, reach, lean, True), shares(number_of, rows * top, reach, lean, False)
    places = jnp.arange(number_of)

    def named(lengths, offset_by):
        used = int((lengths > 0).sum())
        fixed = max(1, used // 4)
        shifted = fixed + (places - fixed + offset_by * (used - fixed)) % max(1, number_of - fixed)
        return jnp.zeros((number_of,), jnp.int32).at[ranking[jnp.where(places < fixed, places, shifted)]].set(jnp.asarray(lengths, jnp.int32))

    lengths = jnp.where(number % 4 == 0, named(crowded, number // 4), named(usual, number - number // 4 - 1))
    mixed = jax.random.permutation(jax.random.fold_in(own, 3), number_of)
    donor, taker = mixed[0:number_of // 2 * 2:2], mixed[1:number_of // 2 * 2:2]
    margin = jnp.minimum(lengths[donor] - 1, reach - lengths[taker]) // 2
    margin = jnp.where((donor == ranking[0]) | (taker == ranking[0]) | (lengths[taker] == 0), 0, jnp.maximum(margin, 0))
    shifted = jax.random.randint(jax.random.fold_in(own, 4), (number_of // 2,), 0, 1 << 20) % (margin + 1)
    lengths = lengths.at[donor].add(-shifted).at[taker].add(shifted)
    labels = jnp.searchsorted(jnp.cumsum(lengths), jnp.arange(rows * top), side="right").astype(jnp.int32)
    grid = labels.reshape(top, rows).T
    grid = grid[jax.random.permutation(jax.random.fold_in(own, 1), rows)]
    offset_by = jax.random.randint(jax.random.fold_in(own, 2), (rows, 1), 0, top)
    return jnp.take_along_axis(grid, (jnp.arange(top)[None, :] + offset_by) % top, axis=1)


def shares(amount, total, most, lean, full):
    weights = [(1 << 20) // math.isqrt(grade ** lean) + 1 for grade in range(1, amount + 1)]
    largest = most if full else min(most, max(-(-total // amount), total * weights[0] // sum(weights)))
    least = 1 if total - largest >= amount - 1 else 0
    counts, surplus = [largest] + [least] * (amount - 1), total - largest - least * (amount - 1)
    while surplus > 0:
        free = [i for i in range(1, amount) if counts[i] < largest] or [i for i in range(1, amount) if counts[i] < most]
        whole, budget = sum([weights[i] for i in free]), surplus
        for i in free:
            more = min(most - counts[i], max(1, budget * weights[i] // whole), surplus)
            counts[i] = counts[i] + more
            surplus = surplus - more
    return np.array(counts)


def scatter_about(own_key, extent, deviation, bound, shards=(), kind=jnp.bfloat16):
    result = jax.random.normal(own_key, extent, jnp.float32) * deviation
    if len(shards) > 0:
        result = steps_of(own_key, extent, shards, -0.22, 0.18) * result
    return jnp.clip(result, min=-bound, max=bound).astype(kind)


def setup_inputs(seed: int = 0) -> dict:
    splits = jax.random.split(jax.random.key(seed), 8)
    section_inputs = scatter_about(splits[0], (2, TOKENS, D), 1.0, 6.0, ((0, 2), (1, 128)))
    output_grads = scatter_about(splits[1], (2, TOKENS, D), 1.0, 6.0, ((0, 2), (1, 128)))
    w_gate = scatter_about(splits[2], (2, D, LIVE * FF), D ** -0.5, 0.0625, ((0, 2), (2, 128)))
    w_up = scatter_about(splits[3], (2, D, LIVE * FF), D ** -0.5, 0.0625, ((0, 2), (2, 128)))
    w_down = scatter_about(splits[4], (2, LIVE * FF, D), FF ** -0.5, 0.125, ((0, 2), (1, 128)))
    route_ids_keys = jax.random.split(jax.random.fold_in(splits[5], 1), 2 * TOKENS // TOK_DEV)
    route_ids_turns = jax.random.permutation(jax.random.fold_in(splits[5], 3), 2 * TOKENS // TOK_DEV)
    route_ids = jax.vmap(lambda own, number: assign_block(jax.random.fold_in(splits[5], 2), own, number, TOK_DEV, EXPERTS, TOPK, CAP, 2))(route_ids_keys, route_ids_turns).reshape((2, TOKENS, TOPK))
    route_gates = jnp.clip(0.25 + 0.75 * jax.random.uniform(splits[6], (2, TOKENS, TOPK), jnp.float32) ** steps_of(splits[6], (2, TOKENS, TOPK), ((0, 2), (1, 128)), -0.2, 0.2), 0.25, 1.0)
    return dict(section_inputs=section_inputs, output_grads=output_grads, w_gate=w_gate, w_up=w_up, w_down=w_down, route_ids=route_ids, route_gates=route_gates)


def one_section(inputs, grads, route, gate, w_gate, w_up, w_down):
    limit = N_EXPERT * CAP
    block_width = FF // SHARDS
    zero_row = jnp.zeros((1, D), jnp.bfloat16)
    inputs_pad = jnp.concatenate([inputs, zero_row], 0)
    grads_pad = jnp.concatenate([grads, zero_row], 0)

    def step(branch, expert):
        hit = route == expert
        chosen = jnp.any(hit, axis=1)
        weight = jnp.sum(jnp.where(hit, gate, jnp.float32(0.0)), axis=1)
        weight_pad = jnp.concatenate([weight, jnp.zeros((1,), jnp.float32)])
        index = jnp.nonzero(chosen, size=limit, fill_value=TOKENS)[0].astype(jnp.int32)
        rows_in = inputs_pad[index]
        rows_grad = (weight_pad[index][:, None] * grads_pad[index].astype(jnp.float32)).astype(jnp.bfloat16)
        start = (expert * FF).astype(jnp.int32)
        gate_cols = lax.dynamic_slice_in_dim(w_gate, start, FF, 1)
        up_cols = lax.dynamic_slice_in_dim(w_up, start, FF, 1)
        down_rows = lax.dynamic_slice_in_dim(w_down, start, FF, 0)
        gate_pre = jnp.dot(rows_in, gate_cols, preferred_element_type=jnp.float32)
        up_pre = jnp.dot(rows_in, up_cols, preferred_element_type=jnp.float32)
        sigma = jax.nn.sigmoid(gate_pre)
        silu_gate = gate_pre * sigma
        hidden = (silu_gate * up_pre).astype(jnp.bfloat16)
        back_hidden = jnp.dot(rows_grad, down_rows.T, preferred_element_type=jnp.float32)
        grad_gate = (back_hidden * up_pre * sigma * (1.0 + gate_pre * (1.0 - sigma))).astype(jnp.bfloat16)
        grad_up = (back_hidden * silu_gate).astype(jnp.bfloat16)
        part_gate = jnp.einsum("lsh,dsh->lsd", grad_gate.astype(jnp.float32).reshape(limit, SHARDS, block_width), gate_cols.astype(jnp.float32).reshape(D, SHARDS, block_width))
        part_up = jnp.einsum("lsh,dsh->lsd", grad_up.astype(jnp.float32).reshape(limit, SHARDS, block_width), up_cols.astype(jnp.float32).reshape(D, SHARDS, block_width))
        rounded = lax.optimization_barrier((part_gate + part_up).astype(jnp.bfloat16))
        summed = jnp.sum(rounded.astype(jnp.float32), axis=1)
        branch = branch.at[index].add(summed)
        down_part = jnp.dot(hidden.T, rows_grad, preferred_element_type=jnp.float32).astype(jnp.bfloat16)
        return branch, down_part

    branch, downs = lax.scan(step, jnp.zeros((TOKENS + 1, D), jnp.float32), jnp.arange(LIVE, dtype=jnp.int32))
    input_grad = (grads.astype(jnp.float32) + branch[:TOKENS]).astype(jnp.bfloat16)
    return input_grad, downs.reshape(LIVE * FF, D)


def reference(section_inputs, output_grads, w_gate, w_up, w_down, route_ids, route_gates):
    first_grad, first_down = one_section(section_inputs[0], output_grads[0], route_ids[0], route_gates[0], w_gate[0], w_up[0], w_down[0])
    second_grad, second_down = one_section(section_inputs[1], output_grads[1], route_ids[1], route_gates[1], w_gate[1], w_up[1], w_down[1])
    handed_grads = jnp.stack([second_grad, first_grad])
    down_grads = jnp.stack([first_down, second_down])
    return (handed_grads, down_grads)
```

```python
import jax
import jax.numpy as jnp
from jax import lax
from jax.sharding import Mesh
from jax.sharding import PartitionSpec as P

SHARDS = 16
CAP = 5


def from_behind(value, axis, steps):
    count = lax.axis_size(axis)
    pairs = [(source, (source + steps) % count) for source in range(count)]
    return lax.ppermute(value, axis, pairs)


def body(section_inputs, output_grads, w_gate, w_up, w_down, route_ids, route_gates):
    inputs = section_inputs[0]
    grads = output_grads[0]
    route = route_ids[0]
    gate = route_gates[0]
    gate_cols = w_gate[0]
    up_cols = w_up[0]
    down_rows = w_down[0]
    tok_rows, model_width = inputs.shape
    block_width = gate_cols.shape[1]
    live_count = lax.axis_size("group")
    slot_count = CAP
    expert_ids = jnp.arange(live_count, dtype=jnp.int32)
    hit = route[:, :, None] == expert_ids
    member = jnp.sum(hit.astype(jnp.int32), axis=1)
    weight = jnp.sum(jnp.where(hit, gate[:, :, None], 0.0), axis=1)
    position = jnp.cumsum(member, axis=0) - member
    slot_ids = jnp.arange(slot_count, dtype=jnp.int32)
    pick = (member[:, :, None] == 1) & (position[:, :, None] == slot_ids)
    pick_mat = pick.astype(jnp.bfloat16).reshape(tok_rows, live_count * slot_count)
    rows_first = (((0,), (0,)), ((), ()))
    rows_in = lax.dot_general(
        pick_mat, inputs, rows_first, preferred_element_type=jnp.float32
    ).astype(jnp.bfloat16)
    chosen_grads = lax.dot_general(pick_mat, grads, rows_first, preferred_element_type=jnp.float32)
    slot_gate = jnp.sum(pick.astype(jnp.float32) * weight[:, :, None], axis=0).reshape(
        live_count * slot_count, 1
    )
    rows_grad = (chosen_grads * slot_gate).astype(jnp.bfloat16)
    send_in = rows_in.reshape(live_count, slot_count, model_width)
    send_grad = rows_grad.reshape(live_count, slot_count, model_width)
    near_in = lax.all_to_all(send_in, "group", 0, 0, tiled=True)
    near_grad = lax.all_to_all(send_grad, "group", 0, 0, tiled=True)
    got_in = lax.all_gather(near_in, "member", axis=0, tiled=False)
    got_grad = lax.all_gather(near_grad, "member", axis=0, tiled=False)
    members = got_in.shape[0]
    flat_in = got_in.reshape(-1, model_width)
    flat_grad = got_grad.reshape(-1, model_width)
    gate_pre = jnp.dot(flat_in, gate_cols, preferred_element_type=jnp.float32)
    up_pre = jnp.dot(flat_in, up_cols, preferred_element_type=jnp.float32)
    sigma = jax.nn.sigmoid(gate_pre)
    silu_gate = gate_pre * sigma
    hidden = (silu_gate * up_pre).astype(jnp.bfloat16)
    contract = (((1,), (1,)), ((), ()))
    back_hidden = lax.dot_general(
        flat_grad, down_rows, contract, preferred_element_type=jnp.float32
    )
    grad_gate = (back_hidden * up_pre * sigma * (1.0 + gate_pre * (1.0 - sigma))).astype(
        jnp.bfloat16
    )
    grad_up = (back_hidden * silu_gate).astype(jnp.bfloat16)
    partial_value = lax.dot_general(
        grad_gate, gate_cols, contract, preferred_element_type=jnp.float32
    )
    partial_value = partial_value + lax.dot_general(
        grad_up, up_cols, contract, preferred_element_type=jnp.float32
    )
    parts = partial_value.astype(jnp.bfloat16).reshape(members, live_count * slot_count, model_width)
    down_part = lax.dot_general(
        hidden, flat_grad, rows_first, preferred_element_type=jnp.float32
    ).astype(jnp.bfloat16)
    blocks = lax.all_to_all(parts, "member", 0, 0, tiled=True)
    summed = jnp.sum(blocks.astype(jnp.float32), axis=0).reshape(live_count, slot_count, model_width)
    returned = lax.all_to_all(summed, "group", 0, 0, tiled=True)
    branch = jnp.dot(
        pick_mat.astype(jnp.float32),
        returned.reshape(live_count * slot_count, model_width),
        preferred_element_type=jnp.float32,
        precision=lax.Precision.HIGHEST,
    )
    input_grad = (grads.astype(jnp.float32) + branch).astype(jnp.bfloat16)
    handed = from_behind(input_grad, "pipe", -1)
    return (handed[None], down_part[None])


def solution(mesh):
    pipe = mesh.shape["pipe"]
    width = mesh.shape["expert"]
    groups = width // SHARDS
    inner = Mesh(mesh.devices.reshape(pipe, groups, SHARDS), ("pipe", "group", "member"))
    rows = P("pipe", ("group", "member"), None)
    cols = P("pipe", None, ("group", "member"))
    return jax.shard_map(
        body,
        mesh=inner,
        in_specs=(rows, rows, cols, cols, rows, rows, rows),
        out_specs=(rows, rows),
        check_vma=False,
    )
```

```python
import jax
import jax.numpy as jnp
from jax import lax
from jax.sharding import Mesh
from jax.sharding import PartitionSpec as P

SHARDS = 16
CAP = 5


def from_behind(value, axis, steps):
    count = lax.axis_size(axis)
    pairs = [(source, (source + steps) % count) for source in range(count)]
    return lax.ppermute(value, axis, pairs)


def body(section_inputs, output_grads, w_gate, w_up, w_down, route_ids, route_gates):
    inputs = section_inputs[0]
    grads = output_grads[0]
    route = route_ids[0]
    gate = route_gates[0]
    gate_cols = w_gate[0]
    up_cols = w_up[0]
    down_rows = w_down[0]
    tok_rows, model_width = inputs.shape
    block_width = gate_cols.shape[1]
    live_count = lax.axis_size("group")
    slot_count = CAP
    expert_ids = jnp.arange(live_count, dtype=jnp.int32)
    hit = route[:, :, None] == expert_ids
    member = jnp.sum(hit.astype(jnp.int32), axis=1)
    weight = jnp.sum(jnp.where(hit, gate[:, :, None], 0.0), axis=1)
    position = jnp.cumsum(member, axis=0) - member
    slot_ids = jnp.arange(slot_count, dtype=jnp.int32)
    pick = (member[:, :, None] == 1) & (position[:, :, None] == slot_ids)
    pick_mat = pick.astype(jnp.bfloat16).reshape(tok_rows, live_count * slot_count)
    rows_first = (((0,), (0,)), ((), ()))
    rows_in = lax.dot_general(
        pick_mat, inputs, rows_first, preferred_element_type=jnp.float32
    ).astype(jnp.bfloat16)
    chosen_grads = lax.dot_general(pick_mat, grads, rows_first, preferred_element_type=jnp.float32)
    slot_gate = jnp.sum(pick.astype(jnp.float32) * weight[:, :, None], axis=0).reshape(
        live_count * slot_count, 1
    )
    rows_grad = (chosen_grads * slot_gate).astype(jnp.bfloat16)
    send_in = rows_in.reshape(live_count, slot_count, model_width)
    send_grad = rows_grad.reshape(live_count, slot_count, model_width)
    near_in = lax.all_to_all(send_in, "group", 0, 0, tiled=True)
    near_grad = lax.all_to_all(send_grad, "group", 0, 0, tiled=True)
    near_rows = live_count * slot_count
    got_in = lax.all_gather(near_in.reshape(near_rows, model_width), "member", axis=0, tiled=True)
    got_grad = lax.all_gather(near_grad.reshape(near_rows, model_width), "member", axis=0, tiled=True)
    gate_slice = lax.all_to_all(gate_cols, "member", 0, 1, tiled=True)
    up_slice = lax.all_to_all(up_cols, "member", 0, 1, tiled=True)
    members = lax.axis_size("member")
    gate_pre = jnp.dot(got_in, gate_cols, preferred_element_type=jnp.float32)
    up_pre = jnp.dot(got_in, up_cols, preferred_element_type=jnp.float32)
    sigma = jax.nn.sigmoid(gate_pre)
    silu_gate = gate_pre * sigma
    hidden = (silu_gate * up_pre).astype(jnp.bfloat16)
    contract = (((1,), (1,)), ((), ()))
    back_hidden = lax.dot_general(
        got_grad, down_rows, contract, preferred_element_type=jnp.float32
    )
    grad_gate = (back_hidden * up_pre * sigma * (1.0 + gate_pre * (1.0 - sigma))).astype(
        jnp.bfloat16
    )
    grad_up = (back_hidden * silu_gate).astype(jnp.bfloat16)
    all_gate = lax.all_gather(grad_gate, "member", axis=1, tiled=True)
    all_up = lax.all_gather(grad_up, "member", axis=1, tiled=True)
    slice_value = lax.dot_general(
        all_gate, gate_slice, contract, preferred_element_type=jnp.float32
    )
    slice_value = slice_value + lax.dot_general(
        all_up, up_slice, contract, preferred_element_type=jnp.float32
    )
    down_part = lax.dot_general(
        hidden, got_grad, rows_first, preferred_element_type=jnp.float32
    ).astype(jnp.bfloat16)
    slice_value = slice_value.reshape(members, near_rows, -1)
    summed = lax.all_to_all(slice_value, "member", 0, 2, tiled=True)
    summed = summed.reshape(live_count, slot_count, model_width)
    returned = lax.all_to_all(summed, "group", 0, 0, tiled=True)
    branch = jnp.dot(
        pick_mat.astype(jnp.float32),
        returned.reshape(live_count * slot_count, model_width),
        preferred_element_type=jnp.float32,
        precision=lax.Precision.HIGHEST,
    )
    input_grad = (grads.astype(jnp.float32) + branch).astype(jnp.bfloat16)
    handed = from_behind(input_grad, "pipe", -1)
    return (handed[None], down_part[None])


def solution(mesh):
    pipe = mesh.shape["pipe"]
    width = mesh.shape["expert"]
    groups = width // SHARDS
    inner = Mesh(mesh.devices.reshape(pipe, groups, SHARDS), ("pipe", "group", "member"))
    rows = P("pipe", ("group", "member"), None)
    cols = P("pipe", None, ("group", "member"))
    return jax.shard_map(
        body,
        mesh=inner,
        in_specs=(rows, rows, cols, cols, rows, rows, rows),
        out_specs=(rows, rows),
        check_vma=False,
    )
```

```python
import jax
import jax.numpy as jnp
from jax import lax
from jax.sharding import Mesh
from jax.sharding import PartitionSpec as P

SHARDS = 16
CAP = 5


def from_behind(value, axis, steps):
    count = lax.axis_size(axis)
    pairs = [(source, (source + steps) % count) for source in range(count)]
    return lax.ppermute(value, axis, pairs)


def body(section_inputs, output_grads, w_gate, w_up, w_down, route_ids, route_gates):
    inputs = section_inputs[0]
    grads = output_grads[0]
    route = route_ids[0]
    gate = route_gates[0]
    gate_cols = w_gate[0]
    up_cols = w_up[0]
    down_rows = w_down[0]
    tok_rows, model_width = inputs.shape
    block_width = gate_cols.shape[1]
    live_count = lax.axis_size("group")
    slot_count = CAP
    expert_ids = jnp.arange(live_count, dtype=jnp.int32)
    hit = route[:, :, None] == expert_ids
    member = jnp.sum(hit.astype(jnp.int32), axis=1)
    weight = jnp.sum(jnp.where(hit, gate[:, :, None], 0.0), axis=1)
    position = jnp.cumsum(member, axis=0) - member
    slot_ids = jnp.arange(slot_count, dtype=jnp.int32)
    pick = (member[:, :, None] == 1) & (position[:, :, None] == slot_ids)
    pick_mat = pick.astype(jnp.bfloat16).reshape(tok_rows, live_count * slot_count)
    rows_first = (((0,), (0,)), ((), ()))
    rows_in = lax.dot_general(
        pick_mat, inputs, rows_first, preferred_element_type=jnp.float32
    ).astype(jnp.bfloat16)
    chosen_grads = lax.dot_general(pick_mat, grads, rows_first, preferred_element_type=jnp.float32)
    slot_gate = jnp.sum(pick.astype(jnp.float32) * weight[:, :, None], axis=0).reshape(
        live_count * slot_count, 1
    )
    rows_grad = (chosen_grads * slot_gate).astype(jnp.bfloat16)
    send = jnp.concatenate(
        [
            rows_in.reshape(live_count, slot_count, model_width),
            rows_grad.reshape(live_count, slot_count, model_width),
        ],
        axis=1,
    )
    near = lax.all_to_all(send, "group", 0, 0, tiled=True)
    near_rows = live_count * slot_count
    near_in = near[:, :slot_count].reshape(near_rows, model_width)
    near_grad = near[:, slot_count:].reshape(near_rows, model_width)
    got_in = lax.all_gather(near_in, "member", axis=0, tiled=True)
    got_grad = lax.all_gather(near_grad, "member", axis=0, tiled=True)
    both_cols = jnp.concatenate([gate_cols, up_cols], axis=1)
    both_slice = lax.all_to_all(both_cols, "member", 0, 1, tiled=True)
    both_slice, got_in = lax.optimization_barrier((both_slice, got_in))
    members = lax.axis_size("member")
    groups = live_count
    gate_pre = jnp.dot(got_in, gate_cols, preferred_element_type=jnp.float32)
    up_pre = jnp.dot(got_in, up_cols, preferred_element_type=jnp.float32)
    sigma = jax.nn.sigmoid(gate_pre)
    silu_gate = gate_pre * sigma
    hidden = (silu_gate * up_pre).astype(jnp.bfloat16)
    contract = (((1,), (1,)), ((), ()))
    back_hidden = lax.dot_general(
        got_grad, down_rows, contract, preferred_element_type=jnp.float32
    )
    grad_gate = (back_hidden * up_pre * sigma * (1.0 + gate_pre * (1.0 - sigma))).astype(
        jnp.bfloat16
    )
    grad_up = (back_hidden * silu_gate).astype(jnp.bfloat16)
    both_grad = jnp.concatenate([grad_gate, grad_up], axis=1)
    all_grad = lax.all_gather(both_grad, "member", axis=1, tiled=True)
    slice_value = lax.dot_general(
        all_grad, both_slice, contract, preferred_element_type=jnp.float32
    )
    down_part = lax.dot_general(
        hidden, got_grad, rows_first, preferred_element_type=jnp.float32
    ).astype(jnp.bfloat16)
    slice_width = slice_value.shape[1]
    slice_value = slice_value.reshape(members, groups, slot_count, slice_width)
    slice_value = jnp.transpose(slice_value, (1, 0, 2, 3)).reshape(
        groups * members, slot_count, slice_width
    )
    back = lax.all_to_all(slice_value, ("group", "member"), 0, 0, tiled=True)
    back = back.reshape(groups, members, slot_count, slice_width)
    returned = jnp.transpose(back, (0, 2, 1, 3)).reshape(groups * slot_count, model_width)
    branch = jnp.dot(
        pick_mat.astype(jnp.float32),
        returned,
        preferred_element_type=jnp.float32,
        precision=lax.Precision.HIGHEST,
    )
    input_grad = (grads.astype(jnp.float32) + branch).astype(jnp.bfloat16)
    handed = from_behind(input_grad, "pipe", -1)
    return (handed[None], down_part[None])


def solution(mesh):
    pipe = mesh.shape["pipe"]
    width = mesh.shape["expert"]
    groups = width // SHARDS
    inner = Mesh(mesh.devices.reshape(pipe, groups, SHARDS), ("pipe", "group", "member"))
    rows = P("pipe", ("group", "member"), None)
    cols = P("pipe", None, ("group", "member"))
    return jax.shard_map(
        body,
        mesh=inner,
        in_specs=(rows, rows, cols, cols, rows, rows, rows),
        out_specs=(rows, rows),
        check_vma=False,
    )
```

```python
import jax
import jax.numpy as jnp
from jax import lax
from jax.sharding import Mesh
from jax.sharding import PartitionSpec as P

SHARDS = 16
CAP = 5


def from_behind(value, axis, steps):
    count = lax.axis_size(axis)
    pairs = [(source, (source + steps) % count) for source in range(count)]
    return lax.ppermute(value, axis, pairs)


def body(section_inputs, output_grads, w_gate, w_up, w_down, route_ids, route_gates):
    inputs = section_inputs[0]
    grads = output_grads[0]
    route = route_ids[0]
    gate = route_gates[0]
    gate_cols = w_gate[0]
    up_cols = w_up[0]
    down_rows = w_down[0]
    tok_rows, model_width = inputs.shape
    block_width = gate_cols.shape[1]
    live_count = lax.axis_size("group")
    slot_count = CAP
    expert_ids = jnp.arange(live_count, dtype=jnp.int32)
    hit = route[:, :, None] == expert_ids
    member = jnp.sum(hit.astype(jnp.int32), axis=1)
    weight = jnp.sum(jnp.where(hit, gate[:, :, None], 0.0), axis=1)
    position = jnp.cumsum(member, axis=0) - member
    slot_ids = jnp.arange(slot_count, dtype=jnp.int32)
    pick = (member[:, :, None] == 1) & (position[:, :, None] == slot_ids)
    pick_mat = pick.astype(jnp.bfloat16).reshape(tok_rows, live_count * slot_count)
    rows_first = (((0,), (0,)), ((), ()))
    rows_in = lax.dot_general(
        pick_mat, inputs, rows_first, preferred_element_type=jnp.float32
    ).astype(jnp.bfloat16)
    chosen_grads = lax.dot_general(pick_mat, grads, rows_first, preferred_element_type=jnp.float32)
    slot_gate = jnp.sum(pick.astype(jnp.float32) * weight[:, :, None], axis=0).reshape(
        live_count * slot_count, 1
    )
    rows_grad = (chosen_grads * slot_gate).astype(jnp.bfloat16)
    both_cols = jnp.concatenate([gate_cols, up_cols], axis=1)
    both_slice = lax.all_to_all(both_cols, "member", 0, 1, tiled=True)
    both_slice, rows_in, rows_grad = lax.optimization_barrier((both_slice, rows_in, rows_grad))
    send = jnp.concatenate(
        [
            rows_in.reshape(live_count, slot_count, model_width),
            rows_grad.reshape(live_count, slot_count, model_width),
        ],
        axis=1,
    )
    near = lax.all_to_all(send, "group", 0, 0, tiled=True)
    near_rows = live_count * slot_count
    near_in = near[:, :slot_count].reshape(near_rows, model_width)
    near_grad = near[:, slot_count:].reshape(near_rows, model_width)
    got_in = lax.all_gather(near_in, "member", axis=0, tiled=True)
    got_grad = lax.all_gather(near_grad, "member", axis=0, tiled=True)
    members = lax.axis_size("member")
    groups = live_count
    gate_pre = jnp.dot(got_in, gate_cols, preferred_element_type=jnp.float32)
    up_pre = jnp.dot(got_in, up_cols, preferred_element_type=jnp.float32)
    sigma = jax.nn.sigmoid(gate_pre)
    silu_gate = gate_pre * sigma
    hidden = (silu_gate * up_pre).astype(jnp.bfloat16)
    contract = (((1,), (1,)), ((), ()))
    back_hidden = lax.dot_general(
        got_grad, down_rows, contract, preferred_element_type=jnp.float32
    )
    grad_gate = (back_hidden * up_pre * sigma * (1.0 + gate_pre * (1.0 - sigma))).astype(
        jnp.bfloat16
    )
    grad_up = (back_hidden * silu_gate).astype(jnp.bfloat16)
    both_grad = jnp.concatenate([grad_gate, grad_up], axis=1)
    all_grad = lax.all_gather(both_grad, "member", axis=1, tiled=True)
    slice_value = lax.dot_general(
        all_grad, both_slice, contract, preferred_element_type=jnp.float32
    )
    down_part = lax.dot_general(
        hidden, got_grad, rows_first, preferred_element_type=jnp.float32
    ).astype(jnp.bfloat16)
    slice_width = slice_value.shape[1]
    slice_value = slice_value.reshape(members, groups, slot_count, slice_width)
    slice_value = jnp.transpose(slice_value, (1, 0, 2, 3)).reshape(
        groups * members, slot_count, slice_width
    )
    back = lax.all_to_all(slice_value, ("group", "member"), 0, 0, tiled=True)
    back = back.reshape(groups, members, slot_count, slice_width)
    returned = jnp.transpose(back, (0, 2, 1, 3)).reshape(groups * slot_count, model_width)
    branch = jnp.dot(
        pick_mat.astype(jnp.float32),
        returned,
        preferred_element_type=jnp.float32,
        precision=lax.Precision.HIGHEST,
    )
    input_grad = (grads.astype(jnp.float32) + branch).astype(jnp.bfloat16)
    handed = from_behind(input_grad, "pipe", -1)
    return (handed[None], down_part[None])


def solution(mesh):
    pipe = mesh.shape["pipe"]
    width = mesh.shape["expert"]
    groups = width // SHARDS
    inner = Mesh(mesh.devices.reshape(pipe, groups, SHARDS), ("pipe", "group", "member"))
    rows = P("pipe", ("group", "member"), None)
    cols = P("pipe", None, ("group", "member"))
    return jax.shard_map(
        body,
        mesh=inner,
        in_specs=(rows, rows, cols, cols, rows, rows, rows),
        out_specs=(rows, rows),
        check_vma=False,
    )
```

```python
import jax
import jax.numpy as jnp
from jax import lax
from jax.sharding import Mesh
from jax.sharding import PartitionSpec as P

SHARDS = 16
CAP = 5


def from_behind(value, axis, steps):
    count = lax.axis_size(axis)
    pairs = [(source, (source + steps) % count) for source in range(count)]
    return lax.ppermute(value, axis, pairs)


def body(section_inputs, output_grads, w_gate, w_up, w_down, route_ids, route_gates):
    inputs = section_inputs[0]
    grads = output_grads[0]
    route = route_ids[0]
    gate = route_gates[0]
    gate_cols = w_gate[0]
    up_cols = w_up[0]
    down_rows = w_down[0]
    tok_rows, model_width = inputs.shape
    block_width = gate_cols.shape[1]
    live_count = lax.axis_size("group")
    slot_count = CAP
    expert_ids = (lax.axis_index("group") + jnp.arange(live_count, dtype=jnp.int32)) % live_count
    hit = route[:, :, None] == expert_ids
    member = jnp.sum(hit.astype(jnp.int32), axis=1)
    weight = jnp.sum(jnp.where(hit, gate[:, :, None], 0.0), axis=1)
    position = jnp.cumsum(member, axis=0) - member
    slot_ids = jnp.arange(slot_count, dtype=jnp.int32)
    pick = (member[:, :, None] == 1) & (position[:, :, None] == slot_ids)
    pick_mat = pick.astype(jnp.bfloat16).reshape(tok_rows, live_count * slot_count)
    rows_first = (((0,), (0,)), ((), ()))
    rows_in = lax.dot_general(
        pick_mat, inputs, rows_first, preferred_element_type=jnp.float32
    ).astype(jnp.bfloat16)
    chosen_grads = lax.dot_general(pick_mat, grads, rows_first, preferred_element_type=jnp.float32)
    slot_gate = jnp.sum(pick.astype(jnp.float32) * weight[:, :, None], axis=0).reshape(
        live_count * slot_count, 1
    )
    rows_grad = (chosen_grads * slot_gate).astype(jnp.bfloat16)
    send = jnp.concatenate(
        [
            rows_in.reshape(live_count, slot_count, model_width),
            rows_grad.reshape(live_count, slot_count, model_width),
        ],
        axis=1,
    )
    near = jnp.stack(
        [send[0]] + [from_behind(send[s], "group", s) for s in range(1, live_count)], axis=0
    )
    near_rows = live_count * slot_count
    near_in = near[:, :slot_count].reshape(near_rows, model_width)
    near_grad = near[:, slot_count:].reshape(near_rows, model_width)
    got_in = lax.all_gather(near_in, "member", axis=0, tiled=True)
    got_grad = lax.all_gather(near_grad, "member", axis=0, tiled=True)
    both_cols = jnp.concatenate([gate_cols, up_cols], axis=1)
    both_slice = lax.all_to_all(both_cols, "member", 0, 1, tiled=True)
    both_slice, got_in = lax.optimization_barrier((both_slice, got_in))
    members = lax.axis_size("member")
    groups = live_count
    gate_pre = jnp.dot(got_in, gate_cols, preferred_element_type=jnp.float32)
    up_pre = jnp.dot(got_in, up_cols, preferred_element_type=jnp.float32)
    sigma = jax.nn.sigmoid(gate_pre)
    silu_gate = gate_pre * sigma
    hidden = (silu_gate * up_pre).astype(jnp.bfloat16)
    contract = (((1,), (1,)), ((), ()))
    back_hidden = lax.dot_general(
        got_grad, down_rows, contract, preferred_element_type=jnp.float32
    )
    grad_gate = (back_hidden * up_pre * sigma * (1.0 + gate_pre * (1.0 - sigma))).astype(
        jnp.bfloat16
    )
    grad_up = (back_hidden * silu_gate).astype(jnp.bfloat16)
    both_grad = jnp.concatenate([grad_gate, grad_up], axis=1)
    all_grad = lax.all_gather(both_grad, "member", axis=1, tiled=True)
    slice_value = lax.dot_general(
        all_grad, both_slice, contract, preferred_element_type=jnp.float32
    )
    down_part = lax.dot_general(
        hidden, got_grad, rows_first, preferred_element_type=jnp.float32
    ).astype(jnp.bfloat16)
    slice_value = slice_value.reshape(members, near_rows, -1)
    summed = lax.all_to_all(slice_value, "member", 0, 2, tiled=True)
    summed = summed.reshape(live_count, slot_count, model_width)
    returned = jnp.concatenate(
        [summed[0]] + [from_behind(summed[s], "group", -s) for s in range(1, live_count)], axis=0
    )
    branch = jnp.dot(
        pick_mat.astype(jnp.float32),
        returned,
        preferred_element_type=jnp.float32,
        precision=lax.Precision.HIGHEST,
    )
    input_grad = (grads.astype(jnp.float32) + branch).astype(jnp.bfloat16)
    handed = from_behind(input_grad, "pipe", -1)
    return (handed[None], down_part[None])


def solution(mesh):
    pipe = mesh.shape["pipe"]
    width = mesh.shape["expert"]
    groups = width // SHARDS
    inner = Mesh(mesh.devices.reshape(pipe, groups, SHARDS), ("pipe", "group", "member"))
    rows = P("pipe", ("group", "member"), None)
    cols = P("pipe", None, ("group", "member"))
    return jax.shard_map(
        body,
        mesh=inner,
        in_specs=(rows, rows, cols, cols, rows, rows, rows),
        out_specs=(rows, rows),
        check_vma=False,
    )
```

```python
import jax
import jax.numpy as jnp
from jax import lax
from jax.sharding import Mesh
from jax.sharding import PartitionSpec as P

SHARDS = 16
CAP = 5


def from_behind(value, axis, steps):
    count = lax.axis_size(axis)
    pairs = [(source, (source + steps) % count) for source in range(count)]
    return lax.ppermute(value, axis, pairs)


def body(section_inputs, output_grads, w_gate, w_up, w_down, route_ids, route_gates):
    inputs = section_inputs[0]
    grads = output_grads[0]
    route = route_ids[0]
    gate = route_gates[0]
    gate_cols = w_gate[0]
    up_cols = w_up[0]
    down_rows = w_down[0]
    tok_rows, model_width = inputs.shape
    block_width = gate_cols.shape[1]
    live_count = lax.axis_size("group")
    slot_count = CAP
    expert_ids = jnp.arange(live_count, dtype=jnp.int32)
    hit = route[:, :, None] == expert_ids
    member = jnp.sum(hit.astype(jnp.int32), axis=1)
    weight = jnp.sum(jnp.where(hit, gate[:, :, None], 0.0), axis=1)
    position = jnp.cumsum(member, axis=0) - member
    slot_ids = jnp.arange(slot_count, dtype=jnp.int32)
    pick = (member[:, :, None] == 1) & (position[:, :, None] == slot_ids)
    pick_mat = pick.astype(jnp.bfloat16).reshape(tok_rows, live_count * slot_count)
    rows_first = (((0,), (0,)), ((), ()))
    rows_in = lax.dot_general(
        pick_mat, inputs, rows_first, preferred_element_type=jnp.float32
    ).astype(jnp.bfloat16)
    chosen_grads = lax.dot_general(pick_mat, grads, rows_first, preferred_element_type=jnp.float32)
    slot_gate = jnp.sum(pick.astype(jnp.float32) * weight[:, :, None], axis=0).reshape(
        live_count * slot_count, 1
    )
    rows_grad = (chosen_grads * slot_gate).astype(jnp.bfloat16)
    send_in = rows_in.reshape(live_count, slot_count, model_width)
    send_grad = rows_grad.reshape(live_count, slot_count, model_width)
    near_rows = live_count * slot_count
    near_in = lax.all_to_all(send_in, "group", 0, 0, tiled=True).reshape(near_rows, model_width)
    near_grad = lax.all_to_all(send_grad, "group", 0, 0, tiled=True).reshape(near_rows, model_width)
    got_in = lax.all_gather(near_in, "member", axis=0, tiled=True)
    got_grad = lax.all_gather(near_grad, "member", axis=0, tiled=True)
    both_cols = jnp.concatenate([gate_cols, up_cols], axis=1)
    both_slice = lax.all_to_all(both_cols, "member", 0, 1, tiled=True)
    both_slice, got_in = lax.optimization_barrier((both_slice, got_in))
    members = lax.axis_size("member")
    groups = live_count
    gate_pre = jnp.dot(got_in, gate_cols, preferred_element_type=jnp.float32)
    up_pre = jnp.dot(got_in, up_cols, preferred_element_type=jnp.float32)
    sigma = jax.nn.sigmoid(gate_pre)
    silu_gate = gate_pre * sigma
    hidden = (silu_gate * up_pre).astype(jnp.bfloat16)
    contract = (((1,), (1,)), ((), ()))
    back_hidden = lax.dot_general(
        got_grad, down_rows, contract, preferred_element_type=jnp.float32
    )
    grad_gate = (back_hidden * up_pre * sigma * (1.0 + gate_pre * (1.0 - sigma))).astype(
        jnp.bfloat16
    )
    grad_up = (back_hidden * silu_gate).astype(jnp.bfloat16)
    both_grad = jnp.concatenate([grad_gate, grad_up], axis=1).T
    all_grad = lax.all_gather(both_grad, "member", axis=0, tiled=True)
    slice_value = lax.dot_general(
        all_grad, both_slice, (((0,), (1,)), ((), ())), preferred_element_type=jnp.float32
    )
    down_part = lax.dot_general(
        hidden, got_grad, rows_first, preferred_element_type=jnp.float32
    ).astype(jnp.bfloat16)
    slice_width = slice_value.shape[1]
    slice_value = slice_value.reshape(members, groups, slot_count, slice_width)
    slice_value = jnp.transpose(slice_value, (1, 0, 2, 3)).reshape(
        groups * members, slot_count, slice_width
    )
    back = lax.all_to_all(slice_value, ("group", "member"), 0, 0, tiled=True)
    back = back.reshape(groups, members, slot_count, slice_width)
    returned = jnp.transpose(back, (0, 2, 1, 3)).reshape(groups * slot_count, model_width)
    branch = jnp.dot(
        pick_mat.astype(jnp.float32),
        returned,
        preferred_element_type=jnp.float32,
        precision=lax.Precision.HIGHEST,
    )
    input_grad = (grads.astype(jnp.float32) + branch).astype(jnp.bfloat16)
    handed = from_behind(input_grad, "pipe", -1)
    return (handed[None], down_part[None])


def solution(mesh):
    pipe = mesh.shape["pipe"]
    width = mesh.shape["expert"]
    groups = width // SHARDS
    inner = Mesh(mesh.devices.reshape(pipe, groups, SHARDS), ("pipe", "group", "member"))
    rows = P("pipe", ("group", "member"), None)
    cols = P("pipe", None, ("group", "member"))
    return jax.shard_map(
        body,
        mesh=inner,
        in_specs=(rows, rows, cols, cols, rows, rows, rows),
        out_specs=(rows, rows),
        check_vma=False,
    )
```

```python
import jax
import jax.numpy as jnp
from jax import lax
from jax.sharding import Mesh
from jax.sharding import PartitionSpec as P

SHARDS = 16
CAP = 5


def from_behind(value, axis, steps):
    count = lax.axis_size(axis)
    pairs = [(source, (source + steps) % count) for source in range(count)]
    return lax.ppermute(value, axis, pairs)


def body(section_inputs, output_grads, w_gate, w_up, w_down, route_ids, route_gates):
    inputs = section_inputs[0]
    grads = output_grads[0]
    route = route_ids[0]
    gate = route_gates[0]
    gate_cols = w_gate[0]
    up_cols = w_up[0]
    down_rows = w_down[0]
    tok_rows, model_width = inputs.shape
    block_width = gate_cols.shape[1]
    live_count = lax.axis_size("group")
    slot_count = CAP
    expert_ids = jnp.arange(live_count, dtype=jnp.int32)
    hit = route[:, :, None] == expert_ids
    member = jnp.sum(hit.astype(jnp.int32), axis=1)
    weight = jnp.sum(jnp.where(hit, gate[:, :, None], 0.0), axis=1)
    position = jnp.cumsum(member, axis=0) - member
    slot_ids = jnp.arange(slot_count, dtype=jnp.int32)
    pick = (member[:, :, None] == 1) & (position[:, :, None] == slot_ids)
    pick_mat = pick.astype(jnp.bfloat16).reshape(tok_rows, live_count * slot_count)
    rows_first = (((0,), (0,)), ((), ()))
    rows_in = lax.dot_general(
        pick_mat, inputs, rows_first, preferred_element_type=jnp.float32
    ).astype(jnp.bfloat16)
    chosen_grads = lax.dot_general(pick_mat, grads, rows_first, preferred_element_type=jnp.float32)
    slot_gate = jnp.sum(pick.astype(jnp.float32) * weight[:, :, None], axis=0).reshape(
        live_count * slot_count, 1
    )
    rows_grad = (chosen_grads * slot_gate).astype(jnp.bfloat16)
    send_in = rows_in.reshape(live_count, slot_count, model_width)
    send_grad = rows_grad.reshape(live_count, slot_count, model_width)
    near_rows = live_count * slot_count
    near_in = lax.all_to_all(send_in, "group", 0, 0, tiled=True).reshape(near_rows, model_width)
    near_grad = lax.all_to_all(send_grad, "group", 0, 0, tiled=True).reshape(near_rows, model_width)
    got_in = lax.all_gather(near_in, "member", axis=0, tiled=True)
    got_grad = lax.all_gather(near_grad, "member", axis=0, tiled=True)
    both_cols = jnp.concatenate([gate_cols, up_cols], axis=1)
    both_cols, got_in, got_grad = lax.optimization_barrier((both_cols, got_in, got_grad))
    both_slice = lax.all_to_all(both_cols, "member", 0, 1, tiled=True)
    members = lax.axis_size("member")
    groups = live_count
    gate_pre = jnp.dot(got_in, gate_cols, preferred_element_type=jnp.float32)
    up_pre = jnp.dot(got_in, up_cols, preferred_element_type=jnp.float32)
    sigma = jax.nn.sigmoid(gate_pre)
    silu_gate = gate_pre * sigma
    hidden = (silu_gate * up_pre).astype(jnp.bfloat16)
    contract = (((1,), (1,)), ((), ()))
    back_hidden = lax.dot_general(
        got_grad, down_rows, contract, preferred_element_type=jnp.float32
    )
    grad_gate = (back_hidden * up_pre * sigma * (1.0 + gate_pre * (1.0 - sigma))).astype(
        jnp.bfloat16
    )
    grad_up = (back_hidden * silu_gate).astype(jnp.bfloat16)
    both_grad = jnp.concatenate([grad_gate, grad_up], axis=1).T
    both_slice, both_grad = lax.optimization_barrier((both_slice, both_grad))
    all_grad = lax.all_gather(both_grad, "member", axis=0, tiled=True)
    slice_value = lax.dot_general(
        all_grad, both_slice, (((0,), (1,)), ((), ())), preferred_element_type=jnp.float32
    )
    down_part = lax.dot_general(
        hidden, got_grad, rows_first, preferred_element_type=jnp.float32
    ).astype(jnp.bfloat16)
    slice_width = slice_value.shape[1]
    slice_value = slice_value.reshape(members, groups, slot_count, slice_width)
    slice_value = jnp.transpose(slice_value, (1, 0, 2, 3)).reshape(
        groups * members, slot_count, slice_width
    )
    back = lax.all_to_all(slice_value.astype(jnp.bfloat16), ("group", "member"), 0, 0, tiled=True)
    back = back.reshape(groups, members, slot_count, slice_width)
    returned = jnp.transpose(back, (0, 2, 1, 3)).reshape(groups * slot_count, model_width)
    returned = returned.astype(jnp.float32)
    branch = jnp.dot(
        pick_mat.astype(jnp.float32),
        returned,
        preferred_element_type=jnp.float32,
        precision=lax.Precision.HIGHEST,
    )
    input_grad = (grads.astype(jnp.float32) + branch).astype(jnp.bfloat16)
    handed = from_behind(input_grad, "pipe", -1)
    return (handed[None], down_part[None])


def solution(mesh):
    pipe = mesh.shape["pipe"]
    width = mesh.shape["expert"]
    groups = width // SHARDS
    inner = Mesh(mesh.devices.reshape(pipe, groups, SHARDS), ("pipe", "group", "member"))
    rows = P("pipe", ("group", "member"), None)
    cols = P("pipe", None, ("group", "member"))
    return jax.shard_map(
        body,
        mesh=inner,
        in_specs=(rows, rows, cols, cols, rows, rows, rows),
        out_specs=(rows, rows),
        check_vma=False,
    )
```

```python
import jax
import jax.numpy as jnp
from jax import lax
from jax.sharding import Mesh
from jax.sharding import PartitionSpec as P

SHARDS = 16
CAP = 5


def from_behind(value, axis, steps):
    count = lax.axis_size(axis)
    pairs = [(source, (source + steps) % count) for source in range(count)]
    return lax.ppermute(value, axis, pairs)


def body(section_inputs, output_grads, w_gate, w_up, w_down, route_ids, route_gates):
    inputs = section_inputs[0]
    grads = output_grads[0]
    route = route_ids[0]
    gate = route_gates[0]
    gate_cols = w_gate[0]
    up_cols = w_up[0]
    down_rows = w_down[0]
    tok_rows, model_width = inputs.shape
    block_width = gate_cols.shape[1]
    live_count = lax.axis_size("group")
    slot_count = CAP
    expert_ids = jnp.arange(live_count, dtype=jnp.int32)
    hit = route[:, :, None] == expert_ids
    member = jnp.sum(hit.astype(jnp.int32), axis=1)
    weight = jnp.sum(jnp.where(hit, gate[:, :, None], 0.0), axis=1)
    position = jnp.cumsum(member, axis=0) - member
    slot_ids = jnp.arange(slot_count, dtype=jnp.int32)
    pick = (member[:, :, None] == 1) & (position[:, :, None] == slot_ids)
    pick_mat = pick.astype(jnp.bfloat16).reshape(tok_rows, live_count * slot_count)
    rows_first = (((0,), (0,)), ((), ()))
    rows_in = lax.dot_general(
        pick_mat, inputs, rows_first, preferred_element_type=jnp.float32
    ).astype(jnp.bfloat16)
    chosen_grads = lax.dot_general(pick_mat, grads, rows_first, preferred_element_type=jnp.float32)
    slot_gate = jnp.sum(pick.astype(jnp.float32) * weight[:, :, None], axis=0).reshape(
        live_count * slot_count, 1
    )
    rows_grad = (chosen_grads * slot_gate).astype(jnp.bfloat16)
    send = jnp.concatenate(
        [
            rows_in.reshape(live_count, slot_count, model_width),
            rows_grad.reshape(live_count, slot_count, model_width),
        ],
        axis=1,
    )
    near = lax.all_to_all(send, "group", 0, 0, tiled=True)
    near_rows = live_count * slot_count
    near = jnp.stack(
        [
            near[:, :slot_count].reshape(near_rows, model_width),
            near[:, slot_count:].reshape(near_rows, model_width),
        ]
    )
    got = lax.all_gather(near, "member", axis=1, tiled=True)
    got_in = got[0]
    got_grad = got[1]
    both_cols = jnp.concatenate([gate_cols, up_cols], axis=1)
    both_cols, got_in, got_grad = lax.optimization_barrier((both_cols, got_in, got_grad))
    both_slice = lax.all_to_all(both_cols, "member", 0, 1, tiled=True)
    members = lax.axis_size("member")
    groups = live_count
    gate_pre = jnp.dot(got_in, gate_cols, preferred_element_type=jnp.float32)
    up_pre = jnp.dot(got_in, up_cols, preferred_element_type=jnp.float32)
    sigma = jax.nn.sigmoid(gate_pre)
    silu_gate = gate_pre * sigma
    hidden = (silu_gate * up_pre).astype(jnp.bfloat16)
    contract = (((1,), (1,)), ((), ()))
    back_hidden = lax.dot_general(
        got_grad, down_rows, contract, preferred_element_type=jnp.float32
    )
    grad_gate = (back_hidden * up_pre * sigma * (1.0 + gate_pre * (1.0 - sigma))).astype(
        jnp.bfloat16
    )
    grad_up = (back_hidden * silu_gate).astype(jnp.bfloat16)
    both_grad = jnp.concatenate([grad_gate, grad_up], axis=1).T
    both_slice, both_grad = lax.optimization_barrier((both_slice, both_grad))
    all_grad = lax.all_gather(both_grad, "member", axis=0, tiled=True)
    slice_value = lax.dot_general(
        all_grad, both_slice, (((0,), (1,)), ((), ())), preferred_element_type=jnp.float32
    )
    down_part = lax.dot_general(
        hidden, got_grad, rows_first, preferred_element_type=jnp.float32
    ).astype(jnp.bfloat16)
    slice_width = slice_value.shape[1]
    slice_value = slice_value.reshape(members, groups, slot_count, slice_width)
    slice_value = jnp.transpose(slice_value, (1, 0, 2, 3)).reshape(
        groups * members, slot_count, slice_width
    )
    back = lax.all_to_all(slice_value.astype(jnp.bfloat16), ("group", "member"), 0, 0, tiled=True)
    back = back.reshape(groups, members, slot_count, slice_width)
    returned = jnp.transpose(back, (0, 2, 1, 3)).reshape(groups * slot_count, model_width)
    returned = returned.astype(jnp.float32)
    branch = jnp.dot(
        pick_mat.astype(jnp.float32),
        returned,
        preferred_element_type=jnp.float32,
        precision=lax.Precision.HIGHEST,
    )
    input_grad = (grads.astype(jnp.float32) + branch).astype(jnp.bfloat16)
    handed = from_behind(input_grad, "pipe", -1)
    return (handed[None], down_part[None])


def solution(mesh):
    pipe = mesh.shape["pipe"]
    width = mesh.shape["expert"]
    groups = width // SHARDS
    inner = Mesh(mesh.devices.reshape(pipe, groups, SHARDS), ("pipe", "group", "member"))
    rows = P("pipe", ("group", "member"), None)
    cols = P("pipe", None, ("group", "member"))
    return jax.shard_map(
        body,
        mesh=inner,
        in_specs=(rows, rows, cols, cols, rows, rows, rows),
        out_specs=(rows, rows),
        check_vma=False,
    )
```

```python
import jax
import jax.numpy as jnp
from jax import lax
from jax.sharding import Mesh
from jax.sharding import PartitionSpec as P

SHARDS = 16
CAP = 5


def from_behind(value, axis, steps):
    count = lax.axis_size(axis)
    pairs = [(source, (source + steps) % count) for source in range(count)]
    return lax.ppermute(value, axis, pairs)


def body(section_inputs, output_grads, w_gate, w_up, w_down, route_ids, route_gates):
    inputs = section_inputs[0]
    grads = output_grads[0]
    route = route_ids[0]
    gate = route_gates[0]
    gate_cols = w_gate[0]
    up_cols = w_up[0]
    down_rows = w_down[0]
    tok_rows, model_width = inputs.shape
    block_width = gate_cols.shape[1]
    live_count = lax.axis_size("group")
    slot_count = CAP
    expert_ids = jnp.arange(live_count, dtype=jnp.int32)
    hit = route[:, :, None] == expert_ids
    member = jnp.sum(hit.astype(jnp.int32), axis=1)
    weight = jnp.sum(jnp.where(hit, gate[:, :, None], 0.0), axis=1)
    position = jnp.cumsum(member, axis=0) - member
    slot_ids = jnp.arange(slot_count, dtype=jnp.int32)
    pick = (member[:, :, None] == 1) & (position[:, :, None] == slot_ids)
    pick_mat = pick.astype(jnp.bfloat16).reshape(tok_rows, live_count * slot_count)
    rows_first = (((0,), (0,)), ((), ()))
    rows_in = lax.dot_general(
        pick_mat, inputs, rows_first, preferred_element_type=jnp.float32
    ).astype(jnp.bfloat16)
    chosen_grads = lax.dot_general(pick_mat, grads, rows_first, preferred_element_type=jnp.float32)
    slot_gate = jnp.sum(pick.astype(jnp.float32) * weight[:, :, None], axis=0).reshape(
        live_count * slot_count, 1
    )
    rows_grad = (chosen_grads * slot_gate).astype(jnp.bfloat16)
    send_in = rows_in.reshape(live_count, slot_count, model_width)
    send_grad = rows_grad.reshape(live_count, slot_count, model_width)
    near_rows = live_count * slot_count
    near_in = lax.all_to_all(send_in, "group", 0, 0, tiled=True).reshape(near_rows, model_width)
    near_grad = lax.all_to_all(send_grad, "group", 0, 0, tiled=True).reshape(near_rows, model_width)
    got_in = lax.all_gather(near_in, "member", axis=0, tiled=True)
    got_grad = lax.all_gather(near_grad, "member", axis=0, tiled=True)
    gate_src, got_in, got_grad = lax.optimization_barrier((gate_cols, got_in, got_grad))
    gate_slice = lax.all_to_all(gate_src, "member", 0, 1, tiled=True)
    up_src, gate_slice = lax.optimization_barrier((up_cols, gate_slice))
    up_slice = lax.all_to_all(up_src, "member", 0, 1, tiled=True)
    members = lax.axis_size("member")
    groups = live_count
    gate_pre = jnp.dot(got_in, gate_cols, preferred_element_type=jnp.float32)
    up_pre = jnp.dot(got_in, up_cols, preferred_element_type=jnp.float32)
    sigma = jax.nn.sigmoid(gate_pre)
    silu_gate = gate_pre * sigma
    hidden = (silu_gate * up_pre).astype(jnp.bfloat16)
    contract = (((1,), (1,)), ((), ()))
    back_hidden = lax.dot_general(
        got_grad, down_rows, contract, preferred_element_type=jnp.float32
    )
    grad_gate = (back_hidden * up_pre * sigma * (1.0 + gate_pre * (1.0 - sigma))).astype(
        jnp.bfloat16
    )
    grad_up = (back_hidden * silu_gate).astype(jnp.bfloat16)
    gate_slice, grad_gate = lax.optimization_barrier((gate_slice, grad_gate.T))
    all_gate = lax.all_gather(grad_gate, "member", axis=0, tiled=True)
    up_slice, grad_up = lax.optimization_barrier((up_slice, grad_up.T))
    all_up = lax.all_gather(grad_up, "member", axis=0, tiled=True)
    grad_first = (((0,), (1,)), ((), ()))
    slice_value = lax.dot_general(
        all_gate, gate_slice, grad_first, preferred_element_type=jnp.float32
    )
    slice_value = slice_value + lax.dot_general(
        all_up, up_slice, grad_first, preferred_element_type=jnp.float32
    )
    down_part = lax.dot_general(
        hidden, got_grad, rows_first, preferred_element_type=jnp.float32
    ).astype(jnp.bfloat16)
    slice_width = slice_value.shape[1]
    slice_value = slice_value.reshape(members, groups, slot_count, slice_width)
    slice_value = jnp.transpose(slice_value, (1, 0, 2, 3)).reshape(
        groups * members, slot_count, slice_width
    )
    back = lax.all_to_all(slice_value.astype(jnp.bfloat16), ("group", "member"), 0, 0, tiled=True)
    back = back.reshape(groups, members, slot_count, slice_width)
    returned = jnp.transpose(back, (0, 2, 1, 3)).reshape(groups * slot_count, model_width)
    returned = returned.astype(jnp.float32)
    branch = jnp.dot(
        pick_mat.astype(jnp.float32),
        returned,
        preferred_element_type=jnp.float32,
        precision=lax.Precision.HIGHEST,
    )
    input_grad = (grads.astype(jnp.float32) + branch).astype(jnp.bfloat16)
    handed = from_behind(input_grad, "pipe", -1)
    return (handed[None], down_part[None])


def solution(mesh):
    pipe = mesh.shape["pipe"]
    width = mesh.shape["expert"]
    groups = width // SHARDS
    inner = Mesh(mesh.devices.reshape(pipe, groups, SHARDS), ("pipe", "group", "member"))
    rows = P("pipe", ("group", "member"), None)
    cols = P("pipe", None, ("group", "member"))
    return jax.shard_map(
        body,
        mesh=inner,
        in_specs=(rows, rows, cols, cols, rows, rows, rows),
        out_specs=(rows, rows),
        check_vma=False,
    )
```

```python
import jax
import jax.numpy as jnp
from jax import lax
from jax.sharding import Mesh
from jax.sharding import PartitionSpec as P

SHARDS = 16
CAP = 5
TILE_ROWS = 16


def from_behind(value, axis, steps):
    count = lax.axis_size(axis)
    pairs = [(source, (source + steps) % count) for source in range(count)]
    return lax.ppermute(value, axis, pairs)


def body(section_inputs, output_grads, w_gate, w_up, w_down, route_ids, route_gates):
    inputs = section_inputs[0]
    grads = output_grads[0]
    route = route_ids[0]
    gate = route_gates[0]
    gate_cols = w_gate[0]
    up_cols = w_up[0]
    down_rows = w_down[0]
    tok_rows, model_width = inputs.shape
    block_width = gate_cols.shape[1]
    live_count = lax.axis_size("group")
    slot_count = CAP
    expert_ids = jnp.arange(live_count, dtype=jnp.int32)
    hit = route[:, :, None] == expert_ids
    member = jnp.sum(hit.astype(jnp.int32), axis=1)
    weight = jnp.sum(jnp.where(hit, gate[:, :, None], 0.0), axis=1)
    position = jnp.cumsum(member, axis=0) - member
    slot_ids = jnp.arange(slot_count, dtype=jnp.int32)
    pick = (member[:, :, None] == 1) & (position[:, :, None] == slot_ids)
    pick_mat = pick.astype(jnp.bfloat16).reshape(tok_rows, live_count * slot_count)
    rows_first = (((0,), (0,)), ((), ()))
    rows_in = lax.dot_general(
        pick_mat, inputs, rows_first, preferred_element_type=jnp.float32
    ).astype(jnp.bfloat16)
    chosen_grads = lax.dot_general(pick_mat, grads, rows_first, preferred_element_type=jnp.float32)
    slot_gate = jnp.sum(pick.astype(jnp.float32) * weight[:, :, None], axis=0).reshape(
        live_count * slot_count, 1
    )
    rows_grad = (chosen_grads * slot_gate).astype(jnp.bfloat16)
    send_in = rows_in.reshape(live_count, TILE_ROWS, -1)
    send_grad = rows_grad.reshape(live_count, TILE_ROWS, -1)
    near_rows = live_count * slot_count
    near_in = lax.all_to_all(send_in, "group", 0, 0, tiled=True).reshape(near_rows, model_width)
    near_grad = lax.all_to_all(send_grad, "group", 0, 0, tiled=True).reshape(near_rows, model_width)
    piece = (2 * TILE_ROWS, -1)
    got_in = lax.all_gather(near_in.reshape(piece), "member", axis=0, tiled=True)
    got_grad = lax.all_gather(near_grad.reshape(piece), "member", axis=0, tiled=True)
    got_in = got_in.reshape(-1, model_width)
    got_grad = got_grad.reshape(-1, model_width)
    both_cols = jnp.concatenate([gate_cols, up_cols], axis=1)
    both_cols, got_in, got_grad = lax.optimization_barrier((both_cols, got_in, got_grad))
    both_slice = lax.all_to_all(both_cols, "member", 0, 1, tiled=True)
    members = lax.axis_size("member")
    groups = live_count
    gate_pre = jnp.dot(got_in, gate_cols, preferred_element_type=jnp.float32)
    up_pre = jnp.dot(got_in, up_cols, preferred_element_type=jnp.float32)
    sigma = jax.nn.sigmoid(gate_pre)
    silu_gate = gate_pre * sigma
    hidden = (silu_gate * up_pre).astype(jnp.bfloat16)
    contract = (((1,), (1,)), ((), ()))
    back_hidden = lax.dot_general(
        got_grad, down_rows, contract, preferred_element_type=jnp.float32
    )
    grad_gate = (back_hidden * up_pre * sigma * (1.0 + gate_pre * (1.0 - sigma))).astype(
        jnp.bfloat16
    )
    grad_up = (back_hidden * silu_gate).astype(jnp.bfloat16)
    both_grad = jnp.concatenate([grad_gate, grad_up], axis=1).T
    both_slice, both_grad = lax.optimization_barrier((both_slice, both_grad))
    grad_rows = both_grad.shape[1]
    all_grad = lax.all_gather(both_grad.reshape(piece), "member", axis=0, tiled=True)
    all_grad = all_grad.reshape(-1, grad_rows)
    slice_value = lax.dot_general(
        all_grad, both_slice, (((0,), (1,)), ((), ())), preferred_element_type=jnp.float32
    )
    down_part = lax.dot_general(
        hidden, got_grad, rows_first, preferred_element_type=jnp.float32
    ).astype(jnp.bfloat16)
    slice_width = slice_value.shape[1]
    slice_value = slice_value.reshape(members, groups, slot_count, slice_width)
    slice_value = jnp.transpose(slice_value, (1, 0, 2, 3)).reshape(
        groups * members, slot_count, slice_width
    )
    slice_value = slice_value.astype(jnp.bfloat16).reshape(groups * members, TILE_ROWS, -1)
    back = lax.all_to_all(slice_value, ("group", "member"), 0, 0, tiled=True)
    back = back.reshape(groups, members, slot_count, slice_width)
    returned = jnp.transpose(back, (0, 2, 1, 3)).reshape(groups * slot_count, model_width)
    returned = returned.astype(jnp.float32)
    branch = jnp.dot(
        pick_mat.astype(jnp.float32),
        returned,
        preferred_element_type=jnp.float32,
        precision=lax.Precision.HIGHEST,
    )
    input_grad = (grads.astype(jnp.float32) + branch).astype(jnp.bfloat16)
    handed = from_behind(input_grad, "pipe", -1)
    return (handed[None], down_part[None])


def solution(mesh):
    pipe = mesh.shape["pipe"]
    width = mesh.shape["expert"]
    groups = width // SHARDS
    inner = Mesh(mesh.devices.reshape(pipe, groups, SHARDS), ("pipe", "group", "member"))
    rows = P("pipe", ("group", "member"), None)
    cols = P("pipe", None, ("group", "member"))
    return jax.shard_map(
        body,
        mesh=inner,
        in_specs=(rows, rows, cols, cols, rows, rows, rows),
        out_specs=(rows, rows),
        check_vma=False,
    )
```

```python
import jax
import jax.numpy as jnp
from jax import lax
from jax.sharding import Mesh
from jax.sharding import PartitionSpec as P

SHARDS = 16
CAP = 5
TILE_ROWS = 16


def from_behind(value, axis, steps):
    count = lax.axis_size(axis)
    pairs = [(source, (source + steps) % count) for source in range(count)]
    return lax.ppermute(value, axis, pairs)


def body(section_inputs, output_grads, w_gate, w_up, w_down, route_ids, route_gates):
    inputs = section_inputs[0]
    grads = output_grads[0]
    route = route_ids[0]
    gate = route_gates[0]
    gate_cols = w_gate[0]
    up_cols = w_up[0]
    down_rows = w_down[0]
    tok_rows, model_width = inputs.shape
    block_width = gate_cols.shape[1]
    live_count = lax.axis_size("group")
    slot_count = CAP
    expert_ids = jnp.arange(live_count, dtype=jnp.int32)
    hit = route[:, :, None] == expert_ids
    member = jnp.sum(hit.astype(jnp.int32), axis=1)
    weight = jnp.sum(jnp.where(hit, gate[:, :, None], 0.0), axis=1)
    position = jnp.cumsum(member, axis=0) - member
    slot_ids = jnp.arange(slot_count, dtype=jnp.int32)
    pick = (member[:, :, None] == 1) & (position[:, :, None] == slot_ids)
    pick_mat = pick.astype(jnp.bfloat16).reshape(tok_rows, live_count * slot_count)
    rows_first = (((0,), (0,)), ((), ()))
    rows_in = lax.dot_general(
        pick_mat, inputs, rows_first, preferred_element_type=jnp.float32
    ).astype(jnp.bfloat16)
    chosen_grads = lax.dot_general(pick_mat, grads, rows_first, preferred_element_type=jnp.float32)
    slot_gate = jnp.sum(pick.astype(jnp.float32) * weight[:, :, None], axis=0).reshape(
        live_count * slot_count, 1
    )
    rows_grad = (chosen_grads * slot_gate).astype(jnp.bfloat16)
    send_in = rows_in.reshape(live_count, TILE_ROWS, -1)
    send_grad = rows_grad.reshape(live_count, TILE_ROWS, -1)
    near_rows = live_count * slot_count
    near_in = lax.all_to_all(send_in, "group", 0, 0, tiled=True).reshape(near_rows, model_width)
    near_grad = lax.all_to_all(send_grad, "group", 0, 0, tiled=True).reshape(near_rows, model_width)
    got_in = lax.all_gather(near_in, "member", axis=0, tiled=True)
    got_grad = lax.all_gather(near_grad, "member", axis=0, tiled=True)
    both_cols = jnp.concatenate([gate_cols, up_cols], axis=1)
    both_cols, got_in, got_grad = lax.optimization_barrier((both_cols, got_in, got_grad))
    both_slice = lax.all_to_all(both_cols, "member", 0, 1, tiled=True)
    members = lax.axis_size("member")
    groups = live_count
    gate_pre = jnp.dot(got_in, gate_cols, preferred_element_type=jnp.float32)
    up_pre = jnp.dot(got_in, up_cols, preferred_element_type=jnp.float32)
    sigma = jax.nn.sigmoid(gate_pre)
    silu_gate = gate_pre * sigma
    hidden = (silu_gate * up_pre).astype(jnp.bfloat16)
    contract = (((1,), (1,)), ((), ()))
    back_hidden = lax.dot_general(
        got_grad, down_rows, contract, preferred_element_type=jnp.float32
    )
    grad_gate = (back_hidden * up_pre * sigma * (1.0 + gate_pre * (1.0 - sigma))).astype(
        jnp.bfloat16
    )
    grad_up = (back_hidden * silu_gate).astype(jnp.bfloat16)
    both_grad = jnp.concatenate([grad_gate, grad_up], axis=1).T
    both_slice, both_grad = lax.optimization_barrier((both_slice, both_grad))
    all_grad = lax.all_gather(both_grad, "member", axis=0, tiled=True)
    slice_value = lax.dot_general(
        all_grad, both_slice, (((0,), (1,)), ((), ())), preferred_element_type=jnp.float32
    )
    down_part = lax.dot_general(
        hidden, got_grad, rows_first, preferred_element_type=jnp.float32
    ).astype(jnp.bfloat16)
    slice_width = slice_value.shape[1]
    slice_value = slice_value.reshape(members, groups, slot_count, slice_width)
    slice_value = jnp.transpose(slice_value, (1, 0, 2, 3)).reshape(
        groups * members, slot_count, slice_width
    )
    back = lax.all_to_all(slice_value.astype(jnp.bfloat16), ("group", "member"), 0, 0, tiled=True)
    back = back.reshape(groups, members, slot_count, slice_width)
    returned = jnp.transpose(back, (0, 2, 1, 3)).reshape(groups * slot_count, model_width)
    returned = returned.astype(jnp.float32)
    branch = jnp.dot(
        pick_mat.astype(jnp.float32),
        returned,
        preferred_element_type=jnp.float32,
        precision=lax.Precision.HIGHEST,
    )
    input_grad = (grads.astype(jnp.float32) + branch).astype(jnp.bfloat16)
    handed = from_behind(input_grad, "pipe", -1)
    return (handed[None], down_part[None])


def solution(mesh):
    pipe = mesh.shape["pipe"]
    width = mesh.shape["expert"]
    groups = width // SHARDS
    inner = Mesh(mesh.devices.reshape(pipe, groups, SHARDS), ("pipe", "group", "member"))
    rows = P("pipe", ("group", "member"), None)
    cols = P("pipe", None, ("group", "member"))
    return jax.shard_map(
        body,
        mesh=inner,
        in_specs=(rows, rows, cols, cols, rows, rows, rows),
        out_specs=(rows, rows),
        check_vma=False,
    )
```

```python
import jax
import jax.numpy as jnp
from jax import lax
from jax.sharding import Mesh
from jax.sharding import PartitionSpec as P

SHARDS = 16
CAP = 5
TILE_ROWS = 16


def from_behind(value, axis, steps):
    count = lax.axis_size(axis)
    pairs = [(source, (source + steps) % count) for source in range(count)]
    return lax.ppermute(value, axis, pairs)


def body(section_inputs, output_grads, w_gate, w_up, w_down, route_ids, route_gates):
    inputs = section_inputs[0]
    grads = output_grads[0]
    route = route_ids[0]
    gate = route_gates[0]
    gate_cols = w_gate[0]
    up_cols = w_up[0]
    down_rows = w_down[0]
    tok_rows, model_width = inputs.shape
    block_width = gate_cols.shape[1]
    live_count = lax.axis_size("group")
    slot_count = CAP
    expert_ids = jnp.arange(live_count, dtype=jnp.int32)
    hit = route[:, :, None] == expert_ids
    member = jnp.sum(hit.astype(jnp.int32), axis=1)
    weight = jnp.sum(jnp.where(hit, gate[:, :, None], 0.0), axis=1)
    position = jnp.cumsum(member, axis=0) - member
    slot_ids = jnp.arange(slot_count, dtype=jnp.int32)
    pick = (member[:, :, None] == 1) & (position[:, :, None] == slot_ids)
    pick_mat = pick.astype(jnp.bfloat16).reshape(tok_rows, live_count * slot_count)
    rows_first = (((0,), (0,)), ((), ()))
    rows_in = lax.dot_general(
        pick_mat, inputs, rows_first, preferred_element_type=jnp.float32
    ).astype(jnp.bfloat16)
    chosen_grads = lax.dot_general(pick_mat, grads, rows_first, preferred_element_type=jnp.float32)
    slot_gate = jnp.sum(pick.astype(jnp.float32) * weight[:, :, None], axis=0).reshape(
        live_count * slot_count, 1
    )
    rows_grad = (chosen_grads * slot_gate).astype(jnp.bfloat16)
    send_in = rows_in.reshape(live_count, TILE_ROWS, -1)
    send_grad = rows_grad.reshape(live_count, TILE_ROWS, -1)
    near_rows = live_count * slot_count
    near_in = lax.all_to_all(send_in, "group", 0, 0, tiled=True).reshape(near_rows, model_width)
    near_grad = lax.all_to_all(send_grad, "group", 0, 0, tiled=True).reshape(near_rows, model_width)
    got_in = lax.all_gather(near_in, "member", axis=0, tiled=True)
    got_grad = lax.all_gather(near_grad, "member", axis=0, tiled=True)
    both_cols = jnp.concatenate([gate_cols, up_cols], axis=1)
    both_cols, got_in, got_grad = lax.optimization_barrier((both_cols, got_in, got_grad))
    both_slice = lax.all_to_all(both_cols, "member", 0, 1, tiled=True)
    members = lax.axis_size("member")
    groups = live_count
    gate_pre = jnp.dot(got_in, gate_cols, preferred_element_type=jnp.float32)
    up_pre = jnp.dot(got_in, up_cols, preferred_element_type=jnp.float32)
    sigma = jax.nn.sigmoid(gate_pre)
    silu_gate = gate_pre * sigma
    hidden = (silu_gate * up_pre).astype(jnp.bfloat16)
    contract = (((1,), (1,)), ((), ()))
    back_hidden = lax.dot_general(
        got_grad, down_rows, contract, preferred_element_type=jnp.float32
    )
    grad_gate = (back_hidden * up_pre * sigma * (1.0 + gate_pre * (1.0 - sigma))).astype(
        jnp.bfloat16
    )
    grad_up = (back_hidden * silu_gate).astype(jnp.bfloat16)
    both_grad = jnp.concatenate([grad_gate, grad_up], axis=1).T
    down_part = lax.dot_general(
        hidden, got_grad, rows_first, preferred_element_type=jnp.float32
    ).astype(jnp.bfloat16)
    both_slice, both_grad, down_part = lax.optimization_barrier((both_slice, both_grad, down_part))
    all_grad = lax.all_gather(both_grad, "member", axis=0, tiled=True)
    slice_value = lax.dot_general(
        all_grad, both_slice, (((0,), (1,)), ((), ())), preferred_element_type=jnp.float32
    )
    slice_width = slice_value.shape[1]
    slice_value = slice_value.reshape(members, groups, slot_count, slice_width)
    slice_value = jnp.transpose(slice_value, (1, 0, 2, 3)).reshape(
        groups * members, slot_count, slice_width
    )
    back = lax.all_to_all(slice_value.astype(jnp.bfloat16), ("group", "member"), 0, 0, tiled=True)
    back = back.reshape(groups, members, slot_count, slice_width)
    returned = jnp.transpose(back, (0, 2, 1, 3)).reshape(groups * slot_count, model_width)
    returned = returned.astype(jnp.float32)
    branch = jnp.dot(
        pick_mat.astype(jnp.float32),
        returned,
        preferred_element_type=jnp.float32,
        precision=lax.Precision.HIGHEST,
    )
    input_grad = (grads.astype(jnp.float32) + branch).astype(jnp.bfloat16)
    handed = from_behind(input_grad, "pipe", -1)
    return (handed[None], down_part[None])


def solution(mesh):
    pipe = mesh.shape["pipe"]
    width = mesh.shape["expert"]
    groups = width // SHARDS
    inner = Mesh(mesh.devices.reshape(pipe, groups, SHARDS), ("pipe", "group", "member"))
    rows = P("pipe", ("group", "member"), None)
    cols = P("pipe", None, ("group", "member"))
    return jax.shard_map(
        body,
        mesh=inner,
        in_specs=(rows, rows, cols, cols, rows, rows, rows),
        out_specs=(rows, rows),
        check_vma=False,
    )
```

```python
import jax
import jax.numpy as jnp
from jax import lax
from jax.sharding import Mesh
from jax.sharding import PartitionSpec as P

SHARDS = 16
CAP = 5
TILE_ROWS = 16


def from_behind(value, axis, steps):
    count = lax.axis_size(axis)
    pairs = [(source, (source + steps) % count) for source in range(count)]
    return lax.ppermute(value, axis, pairs)


def body(section_inputs, output_grads, w_gate, w_up, w_down, route_ids, route_gates):
    inputs = section_inputs[0]
    grads = output_grads[0]
    route = route_ids[0]
    gate = route_gates[0]
    gate_cols = w_gate[0]
    up_cols = w_up[0]
    down_rows = w_down[0]
    tok_rows, model_width = inputs.shape
    block_width = gate_cols.shape[1]
    live_count = lax.axis_size("group")
    slot_count = CAP
    expert_ids = jnp.arange(live_count, dtype=jnp.int32)
    hit = route[:, :, None] == expert_ids
    member = jnp.sum(hit.astype(jnp.int32), axis=1)
    weight = jnp.sum(jnp.where(hit, gate[:, :, None], 0.0), axis=1)
    position = jnp.cumsum(member, axis=0) - member
    slot_ids = jnp.arange(slot_count, dtype=jnp.int32)
    pick = (member[:, :, None] == 1) & (position[:, :, None] == slot_ids)
    pick_mat = pick.astype(jnp.bfloat16).reshape(tok_rows, live_count * slot_count)
    rows_first = (((0,), (0,)), ((), ()))
    rows_in = lax.dot_general(
        pick_mat, inputs, rows_first, preferred_element_type=jnp.float32
    ).astype(jnp.bfloat16)
    chosen_grads = lax.dot_general(pick_mat, grads, rows_first, preferred_element_type=jnp.float32)
    slot_gate = jnp.sum(pick.astype(jnp.float32) * weight[:, :, None], axis=0).reshape(
        live_count * slot_count, 1
    )
    rows_grad = (chosen_grads * slot_gate).astype(jnp.bfloat16)
    send_in = rows_in.reshape(live_count, TILE_ROWS, -1)
    send_grad = rows_grad.reshape(live_count, TILE_ROWS, -1)
    near_rows = live_count * slot_count
    near_in = lax.all_to_all(send_in, "group", 0, 0, tiled=True).reshape(near_rows, model_width)
    near_grad = lax.all_to_all(send_grad, "group", 0, 0, tiled=True).reshape(near_rows, model_width)
    got_in = lax.all_gather(near_in, "member", axis=0, tiled=True)
    got_grad = lax.all_gather(near_grad, "member", axis=0, tiled=True)
    both_cols = jnp.concatenate([gate_cols, up_cols], axis=1)
    both_cols, got_in, got_grad = lax.optimization_barrier((both_cols, got_in, got_grad))
    both_slice = lax.all_to_all(
        both_cols.reshape(SHARDS, -1, both_cols.shape[1]), "member", 0, 0, tiled=True
    )
    members = lax.axis_size("member")
    groups = live_count
    gate_pre = jnp.dot(got_in, gate_cols, preferred_element_type=jnp.float32)
    up_pre = jnp.dot(got_in, up_cols, preferred_element_type=jnp.float32)
    sigma = jax.nn.sigmoid(gate_pre)
    silu_gate = gate_pre * sigma
    hidden = (silu_gate * up_pre).astype(jnp.bfloat16)
    contract = (((1,), (1,)), ((), ()))
    back_hidden = lax.dot_general(
        got_grad, down_rows, contract, preferred_element_type=jnp.float32
    )
    grad_gate = (back_hidden * up_pre * sigma * (1.0 + gate_pre * (1.0 - sigma))).astype(
        jnp.bfloat16
    )
    grad_up = (back_hidden * silu_gate).astype(jnp.bfloat16)
    both_grad = jnp.concatenate([grad_gate, grad_up], axis=1).T
    down_part = lax.dot_general(
        hidden, got_grad, rows_first, preferred_element_type=jnp.float32
    ).astype(jnp.bfloat16)
    both_slice, both_grad, down_part = lax.optimization_barrier((both_slice, both_grad, down_part))
    all_grad = lax.all_gather(both_grad, "member", axis=0, tiled=False)
    slice_value = lax.dot_general(
        all_grad, both_slice, (((0, 1), (0, 2)), ((), ())), preferred_element_type=jnp.float32
    )
    slice_width = slice_value.shape[1]
    slice_value = slice_value.reshape(members, groups, slot_count, slice_width)
    slice_value = jnp.transpose(slice_value, (1, 0, 2, 3)).reshape(
        groups * members, slot_count, slice_width
    )
    back = lax.all_to_all(slice_value.astype(jnp.bfloat16), ("group", "member"), 0, 0, tiled=True)
    back = back.reshape(groups, members, slot_count, slice_width)
    returned = jnp.transpose(back, (0, 2, 1, 3)).reshape(groups * slot_count, model_width)
    returned = returned.astype(jnp.float32)
    branch = jnp.dot(
        pick_mat.astype(jnp.float32),
        returned,
        preferred_element_type=jnp.float32,
        precision=lax.Precision.HIGHEST,
    )
    input_grad = (grads.astype(jnp.float32) + branch).astype(jnp.bfloat16)
    handed = from_behind(input_grad, "pipe", -1)
    return (handed[None], down_part[None])


def solution(mesh):
    pipe = mesh.shape["pipe"]
    width = mesh.shape["expert"]
    groups = width // SHARDS
    inner = Mesh(mesh.devices.reshape(pipe, groups, SHARDS), ("pipe", "group", "member"))
    rows = P("pipe", ("group", "member"), None)
    cols = P("pipe", None, ("group", "member"))
    return jax.shard_map(
        body,
        mesh=inner,
        in_specs=(rows, rows, cols, cols, rows, rows, rows),
        out_specs=(rows, rows),
        check_vma=False,
    )
```

```python
import jax
import jax.numpy as jnp
from jax import lax
from jax.sharding import Mesh
from jax.sharding import PartitionSpec as P

SHARDS = 16
CAP = 5
TILE_ROWS = 16


def from_behind(value, axis, steps):
    count = lax.axis_size(axis)
    pairs = [(source, (source + steps) % count) for source in range(count)]
    return lax.ppermute(value, axis, pairs)


def body(section_inputs, output_grads, w_gate, w_up, w_down, route_ids, route_gates):
    inputs = section_inputs[0]
    grads = output_grads[0]
    route = route_ids[0]
    gate = route_gates[0]
    gate_cols = w_gate[0]
    up_cols = w_up[0]
    down_rows = w_down[0]
    tok_rows, model_width = inputs.shape
    block_width = gate_cols.shape[1]
    live_count = lax.axis_size("group")
    slot_count = CAP
    expert_ids = jnp.arange(live_count, dtype=jnp.int32)
    hit = route[:, :, None] == expert_ids
    member = jnp.sum(hit.astype(jnp.int32), axis=1)
    weight = jnp.sum(jnp.where(hit, gate[:, :, None], 0.0), axis=1)
    position = jnp.cumsum(member, axis=0) - member
    slot_ids = jnp.arange(slot_count, dtype=jnp.int32)
    pick = (member[:, :, None] == 1) & (position[:, :, None] == slot_ids)
    pick_mat = pick.astype(jnp.bfloat16).reshape(tok_rows, live_count * slot_count)
    rows_first = (((0,), (0,)), ((), ()))
    rows_in = lax.dot_general(
        pick_mat, inputs, rows_first, preferred_element_type=jnp.float32
    ).astype(jnp.bfloat16)
    chosen_grads = lax.dot_general(pick_mat, grads, rows_first, preferred_element_type=jnp.float32)
    slot_gate = jnp.sum(pick.astype(jnp.float32) * weight[:, :, None], axis=0).reshape(
        live_count * slot_count, 1
    )
    rows_grad = (chosen_grads * slot_gate).astype(jnp.bfloat16)
    send_in = rows_in.reshape(live_count, TILE_ROWS, -1)
    send_grad = rows_grad.reshape(live_count, TILE_ROWS, -1)
    near_rows = live_count * slot_count
    near_in = lax.all_to_all(send_in, "group", 0, 0, tiled=True).reshape(near_rows, model_width)
    near_grad = lax.all_to_all(send_grad, "group", 0, 0, tiled=True).reshape(near_rows, model_width)
    got_in = lax.all_gather(near_in, "member", axis=0, tiled=True)
    got_grad = lax.all_gather(near_grad, "member", axis=0, tiled=True)
    both_cols = jnp.concatenate([gate_cols, up_cols], axis=1)
    both_cols, got_in, got_grad = lax.optimization_barrier((both_cols, got_in, got_grad))
    both_slice = lax.all_to_all(
        both_cols.reshape(SHARDS, -1, both_cols.shape[1]), "member", 0, 0, tiled=True
    )
    members = lax.axis_size("member")
    groups = live_count
    gate_pre = jnp.dot(got_in, gate_cols, preferred_element_type=jnp.float32)
    up_pre = jnp.dot(got_in, up_cols, preferred_element_type=jnp.float32)
    sigma = jax.nn.sigmoid(gate_pre)
    silu_gate = gate_pre * sigma
    hidden = (silu_gate * up_pre).astype(jnp.bfloat16)
    contract = (((1,), (1,)), ((), ()))
    back_hidden = lax.dot_general(
        got_grad, down_rows, contract, preferred_element_type=jnp.float32
    )
    grad_gate = (back_hidden * up_pre * sigma * (1.0 + gate_pre * (1.0 - sigma))).astype(
        jnp.bfloat16
    )
    grad_up = (back_hidden * silu_gate).astype(jnp.bfloat16)
    both_grad = jnp.concatenate([grad_gate, grad_up], axis=1).T
    down_part = lax.dot_general(
        hidden, got_grad, rows_first, preferred_element_type=jnp.float32
    ).astype(jnp.bfloat16)
    both_slice, both_grad, down_part = lax.optimization_barrier((both_slice, both_grad, down_part))
    all_grad = lax.all_gather(both_grad, "member", axis=0, tiled=False)
    slice_value = lax.dot_general(
        all_grad, both_slice, (((0, 1), (0, 2)), ((), ())), preferred_element_type=jnp.float32
    )
    slice_width = slice_value.shape[1]
    slice_value = slice_value.reshape(members, groups, slot_count, slice_width)
    slice_value = jnp.transpose(slice_value, (1, 0, 2, 3)).reshape(
        groups * members, slot_count, slice_width
    )
    back = lax.all_to_all(slice_value.astype(jnp.bfloat16), ("group", "member"), 0, 0, tiled=True)
    back = back.reshape(groups, members, slot_count, slice_width)
    returned = jnp.transpose(back, (0, 2, 1, 3)).reshape(groups * slot_count, model_width)
    other_grads = from_behind(grads, "pipe", -1)
    other_pick = from_behind(pick_mat, "pipe", -1)
    other_returned = from_behind(returned, "pipe", -1)
    branch = jnp.dot(other_pick, other_returned, preferred_element_type=jnp.float32)
    handed = (other_grads.astype(jnp.float32) + branch).astype(jnp.bfloat16)
    return (handed[None], down_part[None])


def solution(mesh):
    pipe = mesh.shape["pipe"]
    width = mesh.shape["expert"]
    groups = width // SHARDS
    inner = Mesh(mesh.devices.reshape(pipe, groups, SHARDS), ("pipe", "group", "member"))
    rows = P("pipe", ("group", "member"), None)
    cols = P("pipe", None, ("group", "member"))
    return jax.shard_map(
        body,
        mesh=inner,
        in_specs=(rows, rows, cols, cols, rows, rows, rows),
        out_specs=(rows, rows),
        check_vma=False,
    )
```

```python
import jax
import jax.numpy as jnp
from jax import lax
from jax.sharding import Mesh
from jax.sharding import PartitionSpec as P

SHARDS = 16
CAP = 5
TILE_ROWS = 16


def from_behind(value, axis, steps):
    count = lax.axis_size(axis)
    pairs = [(source, (source + steps) % count) for source in range(count)]
    return lax.ppermute(value, axis, pairs)


def body(section_inputs, output_grads, w_gate, w_up, w_down, route_ids, route_gates):
    inputs = section_inputs[0]
    grads = output_grads[0]
    route = route_ids[0]
    gate = route_gates[0]
    gate_cols = w_gate[0]
    up_cols = w_up[0]
    down_rows = w_down[0]
    tok_rows, model_width = inputs.shape
    block_width = gate_cols.shape[1]
    live_count = lax.axis_size("group")
    slot_count = CAP
    expert_ids = jnp.arange(live_count, dtype=jnp.int32)
    hit = route[:, :, None] == expert_ids
    member = jnp.sum(hit.astype(jnp.int32), axis=1)
    weight = jnp.sum(jnp.where(hit, gate[:, :, None], 0.0), axis=1)
    position = jnp.cumsum(member, axis=0) - member
    slot_ids = jnp.arange(slot_count, dtype=jnp.int32)
    pick = (member[:, :, None] == 1) & (position[:, :, None] == slot_ids)
    pick_mat = pick.astype(jnp.bfloat16).reshape(tok_rows, live_count * slot_count)
    rows_first = (((0,), (0,)), ((), ()))
    rows_in = lax.dot_general(
        pick_mat, inputs, rows_first, preferred_element_type=jnp.float32
    ).astype(jnp.bfloat16)
    chosen_grads = lax.dot_general(pick_mat, grads, rows_first, preferred_element_type=jnp.float32)
    slot_gate = jnp.sum(pick.astype(jnp.float32) * weight[:, :, None], axis=0).reshape(
        live_count * slot_count, 1
    )
    rows_grad = (chosen_grads * slot_gate).astype(jnp.bfloat16)
    send_in = rows_in.reshape(live_count, TILE_ROWS, -1)
    send_grad = rows_grad.reshape(live_count, TILE_ROWS, -1)
    near_rows = live_count * slot_count
    near_in = lax.all_to_all(send_in, "group", 0, 0, tiled=True).reshape(near_rows, model_width)
    near_grad = lax.all_to_all(send_grad, "group", 0, 0, tiled=True).reshape(near_rows, model_width)
    got_in = lax.all_gather(near_in, "member", axis=0, tiled=True)
    got_grad = lax.all_gather(near_grad, "member", axis=0, tiled=True)
    both_cols = jnp.concatenate([gate_cols, up_cols], axis=1)
    other_pick = from_behind(pick_mat, "pipe", -1)
    both_cols, got_in, got_grad, other_pick = lax.optimization_barrier(
        (both_cols, got_in, got_grad, other_pick)
    )
    both_slice = lax.all_to_all(
        both_cols.reshape(SHARDS, -1, both_cols.shape[1]), "member", 0, 0, tiled=True
    )
    members = lax.axis_size("member")
    groups = live_count
    gate_pre = jnp.dot(got_in, gate_cols, preferred_element_type=jnp.float32)
    up_pre = jnp.dot(got_in, up_cols, preferred_element_type=jnp.float32)
    sigma = jax.nn.sigmoid(gate_pre)
    silu_gate = gate_pre * sigma
    hidden = (silu_gate * up_pre).astype(jnp.bfloat16)
    contract = (((1,), (1,)), ((), ()))
    back_hidden = lax.dot_general(
        got_grad, down_rows, contract, preferred_element_type=jnp.float32
    )
    grad_gate = (back_hidden * up_pre * sigma * (1.0 + gate_pre * (1.0 - sigma))).astype(
        jnp.bfloat16
    )
    grad_up = (back_hidden * silu_gate).astype(jnp.bfloat16)
    both_grad = jnp.concatenate([grad_gate, grad_up], axis=1).T
    down_part = lax.dot_general(
        hidden, got_grad, rows_first, preferred_element_type=jnp.float32
    ).astype(jnp.bfloat16)
    both_slice, both_grad, down_part = lax.optimization_barrier((both_slice, both_grad, down_part))
    all_grad = lax.all_gather(both_grad, "member", axis=0, tiled=False)
    slice_value = lax.dot_general(
        all_grad, both_slice, (((0, 1), (0, 2)), ((), ())), preferred_element_type=jnp.float32
    )
    slice_width = slice_value.shape[1]
    slice_value = slice_value.reshape(members, groups, slot_count, slice_width)
    slice_value = jnp.transpose(slice_value, (1, 0, 2, 3)).reshape(
        groups * members, slot_count, slice_width
    )
    back = lax.all_to_all(slice_value.astype(jnp.bfloat16), ("group", "member"), 0, 0, tiled=True)
    back = back.reshape(groups, members, slot_count, slice_width)
    returned = jnp.transpose(back, (0, 2, 1, 3)).reshape(groups * slot_count, model_width)
    other_grads = from_behind(grads, "pipe", -1)
    other_returned = from_behind(returned, "pipe", -1)
    branch = jnp.dot(other_pick, other_returned, preferred_element_type=jnp.float32)
    handed = (other_grads.astype(jnp.float32) + branch).astype(jnp.bfloat16)
    return (handed[None], down_part[None])


def solution(mesh):
    pipe = mesh.shape["pipe"]
    width = mesh.shape["expert"]
    groups = width // SHARDS
    inner = Mesh(mesh.devices.reshape(pipe, groups, SHARDS), ("pipe", "group", "member"))
    rows = P("pipe", ("group", "member"), None)
    cols = P("pipe", None, ("group", "member"))
    return jax.shard_map(
        body,
        mesh=inner,
        in_specs=(rows, rows, cols, cols, rows, rows, rows),
        out_specs=(rows, rows),
        check_vma=False,
    )
```
